32 devices in a mesh: row: 8 (over z, y), col: 4 (over x, core).
Axes of the slice: x: 2, y: 2, z: 4, core: 2. Of those that a mesh axis runs over, the one named last changes fastest.
Arguments:
- factor: float32 [4, 8, 256, 1024], P(None, 'row', None, 'col'), may hold values from -0.1875 to 0.1875
- rhs: float32 [4, 8, 256, 4096], P(None, 'row', None, 'col'), may hold values from -6 to 6
- diag_inv: float32 [4, 256, 256], replicated, may hold values from -0.5 to 1.3, as said below
Outputs:
- updated: float32 [4, 8, 256, 4096], P(None, 'row', None, 'col')
The draws below stay inside these ranges and needn't reach their ends.
Inputs may be any that keep to these rules, and one draw needn't show every extreme that they name: Each diag_inv[k] is lower triangular with its diagonal between 0.7 and 1.3.
All inputs are finite; a program needn't handle non-finite values.
Results may differ from the reference program's by a relative error of at most 0.0001.
Values sent between devices are 32-bit elements; how exact they have to be, the bound alone decides.
No kernel may reach another device: no remote copies, remote signals or barrier semaphores. Data moves between devices by JAX's collectives and lax.ppermute only.
A program may use at most 64 MiB of HBM per device.

```python
import math
import jax
import jax.numpy as jnp
from jax import lax

NB = 256
STEPS = 4
BLK_DEV = 4
RHS = 4096
N_ROW = 8


def draw_diag_inv(key, part):
    first, second = jax.random.split(jax.random.fold_in(key, 17))
    below = jnp.clip(jax.random.normal(first, (STEPS, NB, NB), jnp.float32), -4.0, 4.0) * (0.5 / math.sqrt(NB))
    middle = jax.random.uniform(second, (STEPS, NB), jnp.float32, 0.7, 1.3)
    strict = jnp.tril(jnp.ones((NB, NB), jnp.float32), -1)
    identity = jnp.eye(NB, dtype=jnp.float32)
    return below * strict[None] + middle[:, :, None] * identity[None]


def steps_of(key, extent, cuts, low, largest):
    def one(position, parts):
        draws = jax.random.uniform(jax.random.fold_in(jax.random.fold_in(key, 6), position), (parts,), jnp.float32, low / len(cuts), largest / len(cuts))
        return jnp.repeat(jnp.exp(draws), extent[position] // parts).reshape((-1,) + (1,) * (len(extent) - position - 1))

    factor_of = one(*cuts[0])
    for cut in cuts[1:]:
        factor_of = factor_of * one(*cut)
    return factor_of


def bell_draw(rng, extent, width, most, cuts=(), kind=jnp.bfloat16):
    array = jax.random.normal(rng, extent, jnp.float32) * width
    if len(cuts) > 0:
        array = steps_of(rng, extent, cuts, -0.22, 0.18) * array
    return jnp.clip(array, min=-most, max=most).astype(kind)


def setup_inputs(seed: int = 0) -> dict:
    seeds = jax.random.split(jax.random.key(seed), 4)
    factor = bell_draw(seeds[0], (BLK_DEV, N_ROW, NB, STEPS * NB), (STEPS * NB) ** -0.5, 0.1875, ((1, 8), (3, 4)), jnp.float32)
    rhs = bell_draw(seeds[1], (BLK_DEV, N_ROW, NB, RHS), 1.0, 6.0, ((1, 8), (3, 4)), jnp.float32)
    diag_inv = draw_diag_inv(jax.random.fold_in(seeds[3], 71), 0)
    return dict(factor=factor, rhs=rhs, diag_inv=diag_inv)


def reference(factor, rhs, diag_inv):
    work = rhs
    flat_panel = factor.reshape(BLK_DEV * N_ROW * NB, STEPS * NB)
    blocks = (jnp.arange(BLK_DEV, dtype=jnp.int32)[:, None] * N_ROW + jnp.arange(N_ROW, dtype=jnp.int32)[None, :])[:, :, None, None]
    for step in range(STEPS):
        solved = jnp.dot(diag_inv[step], work[0, step], precision=lax.Precision.HIGHEST, preferred_element_type=jnp.float32)
        update = jnp.dot(flat_panel[:, step * NB:(step + 1) * NB], solved, precision=lax.Precision.HIGHEST, preferred_element_type=jnp.float32)
        update = update.reshape(work.shape)
        work = jnp.where(blocks > step, work - update, jnp.where(blocks == step, solved[None, None], work))
    return work
```

```python
import jax
import jax.numpy as jnp
from jax import lax
from jax.sharding import PartitionSpec as P


def matmul(left, right):
    return jnp.dot(left, right, precision=lax.Precision.HIGHEST, preferred_element_type=jnp.float32)


def neighbours(n):
    kinds = [lambda u: u ^ 1, lambda u: u + 2, lambda u: u - 2]
    if n > 8:
        kinds += [lambda u: u + 8, lambda u: u - 8]
    return kinds


def schedule(n, sources):
    have = [set() for _ in range(n)]
    for item, row in sources.items():
        have[row].add(item)
    slots = []
    while any(len(h) < len(sources) for h in have):
        slot, incoming = [], [set() for _ in range(n)]
        for kind in neighbours(n):
            moves = []
            for u in range(n):
                v = kind(u)
                if not 0 <= v < n:
                    continue
                want = sorted(have[u] - have[v] - incoming[v])
                if want:
                    incoming[v].add(want[0])
                    moves.append((u, v, want[0]))
            if moves:
                slot.append(moves)
        for moves in slot:
            for u, v, item in moves:
                have[v].add(item)
        slots.append(slot)
    return slots


def broadcast(held, n, sources, trash):
    position = lax.axis_index("row")
    for slot in schedule(n, sources):
        received = []
        for moves in slot:
            send = [0] * n
            recv = [trash] * n
            for u, v, item in moves:
                send[u] = item
                recv[v] = item
            payload = held[jnp.asarray(send, jnp.int32)[position]]
            got = lax.ppermute(payload, "row", [(u, v) for u, v, _ in moves])
            received.append((jnp.asarray(recv, jnp.int32)[position], got))
        for index, got in received:
            held = lax.dynamic_update_index_in_dim(held, got, index, 0)
    return held


def per_device(factor, rhs, diag_inv):
    n = lax.axis_size("row")
    steps = diag_inv.shape[0]
    nb = rhs.shape[2]
    local_blocks = rhs.shape[0]
    position = lax.axis_index("row")

    held = jnp.zeros((steps + 1, nb, rhs.shape[3]), jnp.float32)
    held = lax.dynamic_update_index_in_dim(held, rhs[0, 0], jnp.minimum(position, steps), 0)
    held = broadcast(held, n, {k: k for k in range(steps)}, steps)

    panel = lax.all_gather(factor, "col", axis=3, tiled=True)

    width = (steps - 1) * nb
    top = jnp.zeros((steps + 1, nb, width), jnp.float32)
    top = lax.dynamic_update_index_in_dim(top, panel[0, 0, :, :width], jnp.minimum(position, steps), 0)
    top = broadcast(top, n, {k: k for k in range(1, steps)}, steps)

    solved = []
    for k in range(steps):
        acc = held[k]
        for j in range(k):
            acc = acc - matmul(top[k, :, j * nb : (j + 1) * nb], solved[j])
        solved.append(matmul(diag_inv[k], acc))
    every = jnp.concatenate(solved, axis=0)
    stacked = jnp.stack(solved)

    flat_panel = panel.reshape(local_blocks * nb, steps * nb)
    update = matmul(flat_panel, every).reshape(rhs.shape)
    work = rhs - update
    blocks = (jnp.arange(local_blocks, dtype=jnp.int32) * n + position)[:, None, None, None]
    mine = stacked[jnp.minimum(position, steps - 1)][None, None]
    return jnp.where(blocks < steps, mine, work)


def solution(mesh):
    return jax.shard_map(
        per_device,
        mesh=mesh,
        in_specs=(P(None, "row", None, "col"), P(None, "row", None, "col"), P()),
        out_specs=P(None, "row", None, "col"),
        check_vma=False,
    )
```

```python
import jax
import jax.numpy as jnp
from jax import lax
from jax.sharding import PartitionSpec as P


def matmul(left, right):
    return jnp.dot(left, right, precision=lax.Precision.HIGHEST, preferred_element_type=jnp.float32)


def neighbours(n):
    kinds = [lambda u: u ^ 1, lambda u: u + 2, lambda u: u - 2]
    if n > 8:
        kinds += [lambda u: u + 8, lambda u: u - 8]
    return kinds


def schedule(n, sources):
    have = [set() for _ in range(n)]
    for item, row in sources.items():
        have[row].add(item)
    slots = []
    while any(len(h) < len(sources) for h in have):
        slot, incoming = [], [set() for _ in range(n)]
        for kind in neighbours(n):
            moves = []
            for u in range(n):
                v = kind(u)
                if not 0 <= v < n:
                    continue
                want = sorted(have[u] - have[v] - incoming[v])
                if want:
                    incoming[v].add(want[0])
                    moves.append((u, v, want[0]))
            if moves:
                slot.append(moves)
        for moves in slot:
            for u, v, item in moves:
                have[v].add(item)
        slots.append(slot)
    return slots


def member(rows, n):
    return jnp.asarray([u in rows for u in range(n)])[lax.axis_index("row")]


def broadcast(own, n, sources):
    items = {k: own for k in sources}
    for slot in schedule(n, sources):
        received = []
        for moves in slot:
            senders = {}
            for u, _, item in moves:
                senders.setdefault(item, []).append(u)
            order = sorted(senders)
            payload = items[order[0]]
            for item in order[1:]:
                payload = jnp.where(member(senders[item], n), items[item], payload)
            got = lax.ppermute(payload, "row", [(u, v) for u, v, _ in moves])
            received.append((moves, got))
        for moves, got in received:
            receivers = {}
            for _, v, item in moves:
                receivers.setdefault(item, []).append(v)
            for item, rows in receivers.items():
                items[item] = jnp.where(member(rows, n), got, items[item])
    return items


def per_device(factor, rhs, diag_inv):
    n = lax.axis_size("row")
    steps = diag_inv.shape[0]
    nb = rhs.shape[2]
    local_blocks = rhs.shape[0]
    position = lax.axis_index("row")

    held = broadcast(rhs[0, 0], n, {k: k for k in range(steps)})

    panel = lax.all_gather(factor, "col", axis=3, tiled=True)

    width = (steps - 1) * nb
    top = broadcast(panel[0, 0, :, :width], n, {k: k for k in range(1, steps)})

    solved = []
    for k in range(steps):
        acc = held[k]
        for j in range(k):
            acc = acc - matmul(top[k][:, j * nb : (j + 1) * nb], solved[j])
        solved.append(matmul(diag_inv[k], acc))
    every = jnp.concatenate(solved, axis=0)
    stacked = jnp.stack(solved)

    flat_panel = panel.reshape(local_blocks * nb, steps * nb)
    update = matmul(flat_panel, every).reshape(rhs.shape)
    work = rhs - update
    blocks = (jnp.arange(local_blocks, dtype=jnp.int32) * n + position)[:, None, None, None]
    mine = stacked[jnp.minimum(position, steps - 1)][None, None]
    return jnp.where(blocks < steps, mine, work)


def solution(mesh):
    return jax.shard_map(
        per_device,
        mesh=mesh,
        in_specs=(P(None, "row", None, "col"), P(None, "row", None, "col"), P()),
        out_specs=P(None, "row", None, "col"),
        check_vma=False,
    )
```

```python
import jax
import jax.numpy as jnp
from jax import lax
from jax.sharding import PartitionSpec as P


def matmul(left, right):
    return jnp.dot(left, right, precision=lax.Precision.HIGHEST, preferred_element_type=jnp.float32)


def neighbours(n):
    kinds = [lambda u: u ^ 1, lambda u: u + 2, lambda u: u - 2]
    if n > 8:
        kinds += [lambda u: u + 8, lambda u: u - 8]
    return kinds


def schedule(n, sources):
    have = [set() for _ in range(n)]
    for item, row in sources.items():
        have[row].add(item)
    slots = []
    while any(len(h) < len(sources) for h in have):
        slot, incoming = [], [set() for _ in range(n)]
        for kind in neighbours(n):
            moves = []
            for u in range(n):
                v = kind(u)
                if not 0 <= v < n:
                    continue
                want = sorted(have[u] - have[v] - incoming[v])
                if want:
                    incoming[v].add(want[0])
                    moves.append((u, v, want[0]))
            if moves:
                slot.append(moves)
        for moves in slot:
            for u, v, item in moves:
                have[v].add(item)
        slots.append(slot)
    return slots


def member(rows, n):
    return jnp.asarray([u in rows for u in range(n)])[lax.axis_index("row")]


def broadcast(own, n, sources):
    items = {k: own for k in sources}
    for slot in schedule(n, sources):
        received = []
        for moves in slot:
            senders = {}
            for u, _, item in moves:
                senders.setdefault(item, []).append(u)
            order = sorted(senders)
            payload = items[order[0]]
            for item in order[1:]:
                payload = jnp.where(member(senders[item], n), items[item], payload)
            got = lax.ppermute(payload, "row", [(u, v) for u, v, _ in moves])
            received.append((moves, got))
        for moves, got in received:
            receivers = {}
            for _, v, item in moves:
                receivers.setdefault(item, []).append(v)
            for item, rows in receivers.items():
                items[item] = jnp.where(member(rows, n), got, items[item])
    return items


def per_device(factor, rhs, diag_inv):
    n = lax.axis_size("row")
    steps = diag_inv.shape[0]
    nb = rhs.shape[2]
    local_blocks = rhs.shape[0]
    position = lax.axis_index("row")

    held = broadcast(rhs[0, 0], n, {k: k for k in range(steps)})

    first = lax.all_gather(factor[:1], "col", axis=3, tiled=True)
    rest = lax.all_gather(factor[1:], "col", axis=3, tiled=True)
    panel = jnp.concatenate([first, rest], axis=0)

    width = (steps - 1) * nb
    top = broadcast(first[0, 0, :, :width], n, {k: k for k in range(1, steps)})

    solved = []
    for k in range(steps):
        acc = held[k]
        for j in range(k):
            acc = acc - matmul(top[k][:, j * nb : (j + 1) * nb], solved[j])
        solved.append(matmul(diag_inv[k], acc))
    every = jnp.concatenate(solved, axis=0)
    stacked = jnp.stack(solved)

    flat_panel = panel.reshape(local_blocks * nb, steps * nb)
    update = matmul(flat_panel, every).reshape(rhs.shape)
    work = rhs - update
    blocks = (jnp.arange(local_blocks, dtype=jnp.int32) * n + position)[:, None, None, None]
    mine = stacked[jnp.minimum(position, steps - 1)][None, None]
    return jnp.where(blocks < steps, mine, work)


def solution(mesh):
    return jax.shard_map(
        per_device,
        mesh=mesh,
        in_specs=(P(None, "row", None, "col"), P(None, "row", None, "col"), P()),
        out_specs=P(None, "row", None, "col"),
        check_vma=False,
    )
```

```python
import jax
import jax.numpy as jnp
from jax import lax
from jax.sharding import PartitionSpec as P


def matmul(left, right):
    return jnp.dot(left, right, precision=lax.Precision.HIGHEST, preferred_element_type=jnp.float32)


def neighbours(n):
    kinds = [lambda u: u ^ 1, lambda u: u + 2, lambda u: u - 2]
    if n > 8:
        kinds += [lambda u: u + 8, lambda u: u - 8]
    return kinds


def schedule(n, sources):
    have = [set() for _ in range(n)]
    for item, row in sources.items():
        have[row].add(item)
    slots = []
    while any(len(h) < len(sources) for h in have):
        slot, incoming = [], [set() for _ in range(n)]
        for kind in neighbours(n):
            moves = []
            for u in range(n):
                v = kind(u)
                if not 0 <= v < n:
                    continue
                want = sorted(have[u] - have[v] - incoming[v])
                if want:
                    incoming[v].add(want[0])
                    moves.append((u, v, want[0]))
            if moves:
                slot.append(moves)
        for moves in slot:
            for u, v, item in moves:
                have[v].add(item)
        slots.append(slot)
    return slots


def member(rows, n):
    position = lax.axis_index("row")
    found = jnp.zeros((), jnp.bool_)
    for low in range(0, n, 32):
        bits = sum(1 << (u - low) for u in rows if low <= u < low + 32)
        if bits:
            shift = jnp.clip(position - low, 0, 31).astype(jnp.uint32)
            hit = ((jnp.uint32(bits) >> shift) & jnp.uint32(1)) == jnp.uint32(1)
            found = found | (hit & (position >= low) & (position < low + 32))
    return found


def broadcast(own, n, sources):
    if n > 8:
        return broadcast_by_item(own, n, sources)
    arrays = [own]
    where_is = [dict() for _ in range(n)]
    for item, row in sources.items():
        where_is[row][item] = 0
    for slot in schedule(n, sources):
        landed = []
        for moves in slot:
            groups = {}
            for u, v, item in moves:
                groups.setdefault(where_is[u][item], []).append((u, v, item))
            for source, group in sorted(groups.items()):
                arrays.append(lax.ppermute(arrays[source], "row", [(u, v) for u, v, _ in group]))
                landed += [(v, item, len(arrays) - 1) for _, v, item in group]
        for v, item, index in landed:
            where_is[v][item] = index
    items = {}
    for item in sources:
        holders = {}
        for row in range(n):
            holders.setdefault(where_is[row][item], []).append(row)
        order = sorted(holders)
        value = arrays[order[0]]
        for index in order[1:]:
            value = jnp.where(member(holders[index], n), arrays[index], value)
        items[item] = value
    return items


def broadcast_by_item(own, n, sources):
    items = {k: own for k in sources}
    for slot in schedule(n, sources):
        received = []
        for moves in slot:
            senders = {}
            for u, _, item in moves:
                senders.setdefault(item, []).append(u)
            order = sorted(senders)
            payload = items[order[0]]
            for item in order[1:]:
                payload = jnp.where(member(senders[item], n), items[item], payload)
            got = lax.ppermute(payload, "row", [(u, v) for u, v, _ in moves])
            received.append((moves, got))
        for moves, got in received:
            receivers = {}
            for _, v, item in moves:
                receivers.setdefault(item, []).append(v)
            for item, rows in receivers.items():
                items[item] = jnp.where(member(rows, n), got, items[item])
    return items


def per_device(factor, rhs, diag_inv):
    n = lax.axis_size("row")
    steps = diag_inv.shape[0]
    nb = rhs.shape[2]
    local_blocks = rhs.shape[0]
    position = lax.axis_index("row")

    held = broadcast(rhs[0, 0], n, {k: k for k in range(steps)})

    first = lax.all_gather(factor[:1], "col", axis=3, tiled=True)
    rest = lax.all_gather(factor[1:], "col", axis=3, tiled=True)
    panel = jnp.concatenate([first, rest], axis=0)

    width = (steps - 1) * nb
    top = broadcast(first[0, 0, :, :width], n, {k: k for k in range(1, steps)})

    solved = []
    for k in range(steps):
        acc = held[k]
        for j in range(k):
            acc = acc - matmul(top[k][:, j * nb : (j + 1) * nb], solved[j])
        solved.append(matmul(diag_inv[k], acc))
    every = jnp.concatenate(solved, axis=0)
    stacked = jnp.stack(solved)

    flat_panel = panel.reshape(local_blocks * nb, steps * nb)
    update = matmul(flat_panel, every).reshape(rhs.shape)
    work = rhs - update
    blocks = (jnp.arange(local_blocks, dtype=jnp.int32) * n + position)[:, None, None, None]
    mine = stacked[jnp.minimum(position, steps - 1)][None, None]
    return jnp.where(blocks < steps, mine, work)


def solution(mesh):
    return jax.shard_map(
        per_device,
        mesh=mesh,
        in_specs=(P(None, "row", None, "col"), P(None, "row", None, "col"), P()),
        out_specs=P(None, "row", None, "col"),
        check_vma=False,
    )
```

```python
import jax
import jax.numpy as jnp
from jax import lax
from jax.sharding import PartitionSpec as P


def matmul(left, right):
    return jnp.dot(left, right, precision=lax.Precision.HIGHEST, preferred_element_type=jnp.float32)


def neighbours(n):
    kinds = [lambda u: u ^ 1, lambda u: u + 2, lambda u: u - 2]
    if n > 8:
        kinds += [lambda u: u + 8, lambda u: u - 8]
    return kinds


def schedule(n, sources):
    have = [set() for _ in range(n)]
    for item, row in sources.items():
        have[row].add(item)
    slots = []
    while any(len(h) < len(sources) for h in have):
        slot, incoming = [], [set() for _ in range(n)]
        for kind in neighbours(n):
            moves = []
            for u in range(n):
                v = kind(u)
                if not 0 <= v < n:
                    continue
                want = sorted(have[u] - have[v] - incoming[v])
                if want:
                    incoming[v].add(want[0])
                    moves.append((u, v, want[0]))
            if moves:
                slot.append(moves)
        for moves in slot:
            for u, v, item in moves:
                have[v].add(item)
        slots.append(slot)
    return slots


def member(rows, n):
    position = lax.axis_index("row")
    found = jnp.zeros((), jnp.bool_)
    for low in range(0, n, 32):
        bits = sum(1 << (u - low) for u in rows if low <= u < low + 32)
        if bits:
            shift = jnp.clip(position - low, 0, 31).astype(jnp.uint32)
            hit = ((jnp.uint32(bits) >> shift) & jnp.uint32(1)) == jnp.uint32(1)
            found = found | (hit & (position >= low) & (position < low + 32))
    return found


def broadcast(own, n, sources):
    items = {k: own for k in sources}
    for slot in schedule(n, sources):
        received = []
        for moves in slot:
            senders = {}
            for u, _, item in moves:
                senders.setdefault(item, []).append(u)
            order = sorted(senders)
            payload = items[order[0]]
            for item in order[1:]:
                payload = jnp.where(member(senders[item], n), items[item], payload)
            got = lax.ppermute(payload, "row", [(u, v) for u, v, _ in moves])
            received.append((moves, got))
        for moves, got in received:
            receivers = {}
            for _, v, item in moves:
                receivers.setdefault(item, []).append(v)
            for item, rows in receivers.items():
                items[item] = jnp.where(member(rows, n), got, items[item])
    return items


def per_device(factor, rhs, diag_inv):
    n = lax.axis_size("row")
    steps = diag_inv.shape[0]
    nb = rhs.shape[2]
    local_blocks = rhs.shape[0]
    position = lax.axis_index("row")

    held = broadcast(rhs[0, 0], n, {k: k for k in range(steps)})

    first = lax.all_gather(factor[:1], "col", axis=3, tiled=True)
    rest = lax.all_gather(factor[1:], "col", axis=3, tiled=True)
    panel = jnp.concatenate([first, rest], axis=0)

    width = (steps - 1) * nb
    top = broadcast(first[0, 0, :, :width], n, {k: k for k in range(1, steps)})

    solved = []
    for k in range(steps):
        acc = held[k]
        for j in range(k):
            acc = acc - matmul(top[k][:, j * nb : (j + 1) * nb], solved[j])
        solved.append(matmul(diag_inv[k], acc))
    every = jnp.concatenate(solved, axis=0)
    stacked = jnp.stack(solved)

    flat_panel = panel.reshape(local_blocks * nb, steps * nb)
    update = matmul(flat_panel, every).reshape(rhs.shape)
    work = rhs - update
    blocks = (jnp.arange(local_blocks, dtype=jnp.int32) * n + position)[:, None, None, None]
    mine = stacked[jnp.minimum(position, steps - 1)][None, None]
    return jnp.where(blocks < steps, mine, work)


def solution(mesh):
    return jax.shard_map(
        per_device,
        mesh=mesh,
        in_specs=(P(None, "row", None, "col"), P(None, "row", None, "col"), P()),
        out_specs=P(None, "row", None, "col"),
        check_vma=False,
    )
```

```python
import jax
import jax.numpy as jnp
from jax import lax
from jax.sharding import PartitionSpec as P


def matmul(left, right):
    return jnp.dot(left, right, precision=lax.Precision.HIGH, preferred_element_type=jnp.float32)


def neighbours(n):
    kinds = [lambda u: u ^ 1, lambda u: u + 2, lambda u: u - 2]
    if n > 8:
        kinds += [lambda u: u + 8, lambda u: u - 8]
    return kinds


def schedule(n, sources):
    have = [set() for _ in range(n)]
    for item, row in sources.items():
        have[row].add(item)
    slots = []
    while any(len(h) < len(sources) for h in have):
        slot, incoming = [], [set() for _ in range(n)]
        for kind in neighbours(n):
            moves = []
            for u in range(n):
                v = kind(u)
                if not 0 <= v < n:
                    continue
                want = sorted(have[u] - have[v] - incoming[v])
                if want:
                    incoming[v].add(want[0])
                    moves.append((u, v, want[0]))
            if moves:
                slot.append(moves)
        for moves in slot:
            for u, v, item in moves:
                have[v].add(item)
        slots.append(slot)
    return slots


def member(rows, n):
    position = lax.axis_index("row")
    found = jnp.zeros((), jnp.bool_)
    for low in range(0, n, 32):
        bits = sum(1 << (u - low) for u in rows if low <= u < low + 32)
        if bits:
            shift = jnp.clip(position - low, 0, 31).astype(jnp.uint32)
            hit = ((jnp.uint32(bits) >> shift) & jnp.uint32(1)) == jnp.uint32(1)
            found = found | (hit & (position >= low) & (position < low + 32))
    return found


def broadcast(own, n, sources):
    items = {k: own for k in sources}
    for slot in schedule(n, sources):
        received = []
        for moves in slot:
            senders = {}
            for u, _, item in moves:
                senders.setdefault(item, []).append(u)
            order = sorted(senders)
            payload = items[order[0]]
            for item in order[1:]:
                payload = jnp.where(member(senders[item], n), items[item], payload)
            got = lax.ppermute(payload, "row", [(u, v) for u, v, _ in moves])
            received.append((moves, got))
        for moves, got in received:
            receivers = {}
            for _, v, item in moves:
                receivers.setdefault(item, []).append(v)
            for item, rows in receivers.items():
                items[item] = jnp.where(member(rows, n), got, items[item])
    return items


def per_device(factor, rhs, diag_inv):
    n = lax.axis_size("row")
    steps = diag_inv.shape[0]
    nb = rhs.shape[2]
    local_blocks = rhs.shape[0]
    position = lax.axis_index("row")

    held = broadcast(rhs[0, 0], n, {k: k for k in range(steps)})

    first = lax.all_gather(factor[:1], "col", axis=3, tiled=True)
    rest = lax.all_gather(factor[1:], "col", axis=3, tiled=True)
    panel = jnp.concatenate([first, rest], axis=0)

    width = (steps - 1) * nb
    top = broadcast(first[0, 0, :, :width], n, {k: k for k in range(1, steps)})

    solved = []
    for k in range(steps):
        acc = held[k]
        for j in range(k):
            acc = acc - matmul(top[k][:, j * nb : (j + 1) * nb], solved[j])
        solved.append(matmul(diag_inv[k], acc))
    every = jnp.concatenate(solved, axis=0)
    stacked = jnp.stack(solved)

    flat_panel = panel.reshape(local_blocks * nb, steps * nb)
    update = matmul(flat_panel, every).reshape(rhs.shape)
    work = rhs - update
    blocks = (jnp.arange(local_blocks, dtype=jnp.int32) * n + position)[:, None, None, None]
    mine = stacked[jnp.minimum(position, steps - 1)][None, None]
    return jnp.where(blocks < steps, mine, work)


def solution(mesh):
    return jax.shard_map(
        per_device,
        mesh=mesh,
        in_specs=(P(None, "row", None, "col"), P(None, "row", None, "col"), P()),
        out_specs=P(None, "row", None, "col"),
        check_vma=False,
    )
```

```python
import jax
import jax.numpy as jnp
from jax import lax
from jax.sharding import PartitionSpec as P


def matmul(left, right):
    return jnp.dot(left, right, precision=lax.Precision.HIGHEST, preferred_element_type=jnp.float32)


def neighbours(n):
    kinds = [lambda u: u ^ 1, lambda u: u + 2, lambda u: u - 2]
    if n > 8:
        kinds += [lambda u: u + 8, lambda u: u - 8]
    return kinds


def schedule(n, sources):
    have = [set() for _ in range(n)]
    for item, row in sources.items():
        have[row].add(item)
    slots = []
    while any(len(h) < len(sources) for h in have):
        slot, incoming = [], [set() for _ in range(n)]
        for kind in neighbours(n):
            moves = []
            for u in range(n):
                v = kind(u)
                if not 0 <= v < n:
                    continue
                want = sorted(have[u] - have[v] - incoming[v])
                if want:
                    incoming[v].add(want[0])
                    moves.append((u, v, want[0]))
            if moves:
                slot.append(moves)
        for moves in slot:
            for u, v, item in moves:
                have[v].add(item)
        slots.append(slot)
    return slots


def member(rows, n):
    position = lax.axis_index("row")
    found = jnp.zeros((), jnp.bool_)
    for low in range(0, n, 32):
        bits = sum(1 << (u - low) for u in rows if low <= u < low + 32)
        if bits:
            shift = jnp.clip(position - low, 0, 31).astype(jnp.uint32)
            hit = ((jnp.uint32(bits) >> shift) & jnp.uint32(1)) == jnp.uint32(1)
            found = found | (hit & (position >= low) & (position < low + 32))
    return found


def broadcast(own, n, sources):
    items = {k: own for k in sources}
    for slot in schedule(n, sources):
        received = []
        for moves in slot:
            senders = {}
            for u, _, item in moves:
                senders.setdefault(item, []).append(u)
            order = sorted(senders)
            payload = items[order[0]]
            for item in order[1:]:
                payload = jnp.where(member(senders[item], n), items[item], payload)
            got = lax.ppermute(payload, "row", [(u, v) for u, v, _ in moves])
            received.append((moves, got))
        for moves, got in received:
            receivers = {}
            for _, v, item in moves:
                receivers.setdefault(item, []).append(v)
            for item, rows in receivers.items():
                items[item] = jnp.where(member(rows, n), got, items[item])
    return items


def per_device(factor, rhs, diag_inv):
    n = lax.axis_size("row")
    steps = diag_inv.shape[0]
    nb = rhs.shape[2]
    local_blocks = rhs.shape[0]
    position = lax.axis_index("row")

    held = broadcast(rhs[0, 0], n, {k: k for k in range(steps)})

    first = lax.all_gather(factor[:1], "col", axis=3, tiled=True)
    rest = lax.all_gather(factor[1:], "col", axis=3, tiled=True)
    panel = jnp.concatenate([first, rest], axis=0)

    width = (steps - 1) * nb
    cols = lax.axis_size("col")
    if cols % 2 == 0:
        half = nb // 2
        odd = lax.axis_index("col") % 2
        start = (odd * half).astype(jnp.int32)
        mine = lax.dynamic_slice_in_dim(first[0, 0, :, :width], start, half, 0)
        part = broadcast(mine, n, {k: k for k in range(1, steps)})
        pieces = jnp.stack([part[k] for k in range(1, steps)])
        other = lax.ppermute(pieces, "col", [(c, c ^ 1) for c in range(cols)])
        low = jnp.where(odd == 0, pieces, other)
        high = jnp.where(odd == 0, other, pieces)
        joined = jnp.concatenate([low, high], axis=1)
        top = {k: joined[k - 1] for k in range(1, steps)}
    else:
        top = broadcast(first[0, 0, :, :width], n, {k: k for k in range(1, steps)})

    solved = []
    for k in range(steps):
        acc = held[k]
        for j in range(k):
            acc = acc - matmul(top[k][:, j * nb : (j + 1) * nb], solved[j])
        solved.append(matmul(diag_inv[k], acc))
    every = jnp.concatenate(solved, axis=0)
    stacked = jnp.stack(solved)

    flat_panel = panel.reshape(local_blocks * nb, steps * nb)
    update = matmul(flat_panel, every).reshape(rhs.shape)
    work = rhs - update
    blocks = (jnp.arange(local_blocks, dtype=jnp.int32) * n + position)[:, None, None, None]
    mine = stacked[jnp.minimum(position, steps - 1)][None, None]
    return jnp.where(blocks < steps, mine, work)


def solution(mesh):
    return jax.shard_map(
        per_device,
        mesh=mesh,
        in_specs=(P(None, "row", None, "col"), P(None, "row", None, "col"), P()),
        out_specs=P(None, "row", None, "col"),
        check_vma=False,
    )
```

```python
import jax
import jax.numpy as jnp
from jax import lax
from jax.sharding import PartitionSpec as P


def matmul(left, right, precision=lax.Precision.HIGHEST):
    return jnp.dot(left, right, precision=precision, preferred_element_type=jnp.float32)


def neighbours(n):
    kinds = [lambda u: u ^ 1, lambda u: u + 2, lambda u: u - 2]
    if n > 8:
        kinds += [lambda u: u + 8, lambda u: u - 8]
    return kinds


def schedule(n, sources):
    have = [set() for _ in range(n)]
    for item, row in sources.items():
        have[row].add(item)
    slots = []
    while any(len(h) < len(sources) for h in have):
        slot, incoming = [], [set() for _ in range(n)]
        for kind in neighbours(n):
            moves = []
            for u in range(n):
                v = kind(u)
                if not 0 <= v < n:
                    continue
                want = sorted(have[u] - have[v] - incoming[v])
                if want:
                    incoming[v].add(want[0])
                    moves.append((u, v, want[0]))
            if moves:
                slot.append(moves)
        for moves in slot:
            for u, v, item in moves:
                have[v].add(item)
        slots.append(slot)
    return slots


def member(rows, n):
    position = lax.axis_index("row")
    found = jnp.zeros((), jnp.bool_)
    for low in range(0, n, 32):
        bits = sum(1 << (u - low) for u in rows if low <= u < low + 32)
        if bits:
            shift = jnp.clip(position - low, 0, 31).astype(jnp.uint32)
            hit = ((jnp.uint32(bits) >> shift) & jnp.uint32(1)) == jnp.uint32(1)
            found = found | (hit & (position >= low) & (position < low + 32))
    return found


def broadcast(own, n, sources):
    items = {k: own for k in sources}
    for slot in schedule(n, sources):
        received = []
        for moves in slot:
            senders = {}
            for u, _, item in moves:
                senders.setdefault(item, []).append(u)
            order = sorted(senders)
            payload = items[order[0]]
            for item in order[1:]:
                payload = jnp.where(member(senders[item], n), items[item], payload)
            got = lax.ppermute(payload, "row", [(u, v) for u, v, _ in moves])
            received.append((moves, got))
        for moves, got in received:
            receivers = {}
            for _, v, item in moves:
                receivers.setdefault(item, []).append(v)
            for item, rows in receivers.items():
                items[item] = jnp.where(member(rows, n), got, items[item])
    return items


def per_device(factor, rhs, diag_inv):
    n = lax.axis_size("row")
    steps = diag_inv.shape[0]
    nb = rhs.shape[2]
    local_blocks = rhs.shape[0]
    position = lax.axis_index("row")

    held = broadcast(rhs[0, 0], n, {k: k for k in range(steps)})

    first = lax.all_gather(factor[:1], "col", axis=3, tiled=True)
    rest = lax.all_gather(factor[1:], "col", axis=3, tiled=True)
    panel = jnp.concatenate([first, rest], axis=0)

    width = (steps - 1) * nb
    top = broadcast(first[0, 0, :, :width], n, {k: k for k in range(1, steps)})

    solved = []
    for k in range(steps):
        acc = held[k]
        for j in range(k):
            acc = acc - matmul(top[k][:, j * nb : (j + 1) * nb], solved[j])
        solved.append(matmul(diag_inv[k], acc))
    every = jnp.concatenate(solved, axis=0)
    stacked = jnp.stack(solved)

    flat_panel = panel.reshape(local_blocks * nb, steps * nb)
    update = matmul(flat_panel, every, lax.Precision.HIGH).reshape(rhs.shape)
    work = rhs - update
    blocks = (jnp.arange(local_blocks, dtype=jnp.int32) * n + position)[:, None, None, None]
    mine = stacked[jnp.minimum(position, steps - 1)][None, None]
    return jnp.where(blocks < steps, mine, work)


def solution(mesh):
    return jax.shard_map(
        per_device,
        mesh=mesh,
        in_specs=(P(None, "row", None, "col"), P(None, "row", None, "col"), P()),
        out_specs=P(None, "row", None, "col"),
        check_vma=False,
    )
```

```python
import jax
import jax.numpy as jnp
from jax import lax
from jax.sharding import PartitionSpec as P


def matmul(left, right, precision=lax.Precision.HIGHEST):
    return jnp.dot(left, right, precision=precision, preferred_element_type=jnp.float32)


def neighbours(n):
    kinds = [lambda u: u ^ 1, lambda u: u + 2, lambda u: u - 2]
    if n > 8:
        kinds += [lambda u: u + 8, lambda u: u - 8]
    return kinds


def schedule(n, sources):
    have = [set() for _ in range(n)]
    for item, row in sources.items():
        have[row].add(item)
    slots = []
    while any(len(h) < len(sources) for h in have):
        slot, incoming = [], [set() for _ in range(n)]
        for kind in neighbours(n):
            moves = []
            for u in range(n):
                v = kind(u)
                if not 0 <= v < n:
                    continue
                want = sorted(have[u] - have[v] - incoming[v])
                if want:
                    incoming[v].add(want[0])
                    moves.append((u, v, want[0]))
            if moves:
                slot.append(moves)
        for moves in slot:
            for u, v, item in moves:
                have[v].add(item)
        slots.append(slot)
    return slots


def member(rows, n):
    position = lax.axis_index("row")
    found = jnp.zeros((), jnp.bool_)
    for low in range(0, n, 32):
        bits = sum(1 << (u - low) for u in rows if low <= u < low + 32)
        if bits:
            shift = jnp.clip(position - low, 0, 31).astype(jnp.uint32)
            hit = ((jnp.uint32(bits) >> shift) & jnp.uint32(1)) == jnp.uint32(1)
            found = found | (hit & (position >= low) & (position < low + 32))
    return found


def broadcast(own, n, sources):
    items = {k: own for k in sources}
    for slot in schedule(n, sources):
        received = []
        for moves in slot:
            senders = {}
            for u, _, item in moves:
                senders.setdefault(item, []).append(u)
            order = sorted(senders)
            payload = items[order[0]]
            for item in order[1:]:
                payload = jnp.where(member(senders[item], n), items[item], payload)
            got = lax.ppermute(payload, "row", [(u, v) for u, v, _ in moves])
            received.append((moves, got))
        for moves, got in received:
            receivers = {}
            for _, v, item in moves:
                receivers.setdefault(item, []).append(v)
            for item, rows in receivers.items():
                items[item] = jnp.where(member(rows, n), got, items[item])
    return items


def gather_columns(block):
    cols = lax.axis_size("col")
    if cols & (cols - 1):
        return lax.all_gather(block, "col", axis=3, tiled=True)
    index = lax.axis_index("col")
    bit = 1
    while bit < cols:
        other = lax.ppermute(block, "col", [(c, c ^ bit) for c in range(cols)])
        low = (index & bit) == 0
        block = jnp.where(low, jnp.concatenate([block, other], axis=3), jnp.concatenate([other, block], axis=3))
        bit *= 2
    return block


def per_device(factor, rhs, diag_inv):
    n = lax.axis_size("row")
    steps = diag_inv.shape[0]
    nb = rhs.shape[2]
    local_blocks = rhs.shape[0]
    position = lax.axis_index("row")

    held = broadcast(rhs[0, 0], n, {k: k for k in range(steps)})

    first = gather_columns(factor[:1])
    rest = lax.all_gather(factor[1:], "col", axis=3, tiled=True)
    panel = jnp.concatenate([first, rest], axis=0)

    width = (steps - 1) * nb
    top = broadcast(first[0, 0, :, :width], n, {k: k for k in range(1, steps)})

    solved = []
    for k in range(steps):
        acc = held[k]
        for j in range(k):
            acc = acc - matmul(top[k][:, j * nb : (j + 1) * nb], solved[j])
        solved.append(matmul(diag_inv[k], acc))
    every = jnp.concatenate(solved, axis=0)
    stacked = jnp.stack(solved)

    flat_panel = panel.reshape(local_blocks * nb, steps * nb)
    update = matmul(flat_panel, every, lax.Precision.HIGH).reshape(rhs.shape)
    work = rhs - update
    blocks = (jnp.arange(local_blocks, dtype=jnp.int32) * n + position)[:, None, None, None]
    mine = stacked[jnp.minimum(position, steps - 1)][None, None]
    return jnp.where(blocks < steps, mine, work)


def solution(mesh):
    return jax.shard_map(
        per_device,
        mesh=mesh,
        in_specs=(P(None, "row", None, "col"), P(None, "row", None, "col"), P()),
        out_specs=P(None, "row", None, "col"),
        check_vma=False,
    )
```

```python
import jax
import jax.numpy as jnp
from jax import lax
from jax.sharding import PartitionSpec as P


def matmul(left, right, precision=lax.Precision.HIGHEST):
    return jnp.dot(left, right, precision=precision, preferred_element_type=jnp.float32)


def neighbours(n):
    kinds = [lambda u: u ^ 1, lambda u: u + 2, lambda u: u - 2]
    if n > 8:
        kinds += [lambda u: u + 8, lambda u: u - 8]
    return kinds


def schedule(n, sources):
    have = [set() for _ in range(n)]
    for item, row in sources.items():
        have[row].add(item)
    slots = []
    while any(len(h) < len(sources) for h in have):
        slot, incoming = [], [set() for _ in range(n)]
        for kind in neighbours(n):
            moves = []
            for u in range(n):
                v = kind(u)
                if not 0 <= v < n:
                    continue
                want = sorted(have[u] - have[v] - incoming[v])
                if want:
                    incoming[v].add(want[0])
                    moves.append((u, v, want[0]))
            if moves:
                slot.append(moves)
        for moves in slot:
            for u, v, item in moves:
                have[v].add(item)
        slots.append(slot)
    return slots


def member(rows, n):
    position = lax.axis_index("row")
    found = jnp.zeros((), jnp.bool_)
    for low in range(0, n, 32):
        bits = sum(1 << (u - low) for u in rows if low <= u < low + 32)
        if bits:
            shift = jnp.clip(position - low, 0, 31).astype(jnp.uint32)
            hit = ((jnp.uint32(bits) >> shift) & jnp.uint32(1)) == jnp.uint32(1)
            found = found | (hit & (position >= low) & (position < low + 32))
    return found


def broadcast_halves(own, n, rows):
    half = own.shape[1] // 2
    pieces = broadcast(
        {(k, h): own[:, h * half : (h + 1) * half] for k in rows for h in range(2)},
        n,
        {(k, h): rows[k] for k in rows for h in range(2)},
    )
    return {k: jnp.concatenate([pieces[(k, 0)], pieces[(k, 1)]], axis=1) for k in rows}


def broadcast(own, n, sources):
    items = dict(own)
    for slot in schedule(n, sources):
        received = []
        for moves in slot:
            senders = {}
            for u, _, item in moves:
                senders.setdefault(item, []).append(u)
            order = sorted(senders)
            payload = items[order[0]]
            for item in order[1:]:
                payload = jnp.where(member(senders[item], n), items[item], payload)
            got = lax.ppermute(payload, "row", [(u, v) for u, v, _ in moves])
            received.append((moves, got))
        for moves, got in received:
            receivers = {}
            for _, v, item in moves:
                receivers.setdefault(item, []).append(v)
            for item, rows in receivers.items():
                items[item] = jnp.where(member(rows, n), got, items[item])
    return items


def per_device(factor, rhs, diag_inv):
    n = lax.axis_size("row")
    steps = diag_inv.shape[0]
    nb = rhs.shape[2]
    local_blocks = rhs.shape[0]
    position = lax.axis_index("row")

    held = broadcast_halves(rhs[0, 0], n, {k: k for k in range(steps)})

    first = lax.all_gather(factor[:1], "col", axis=3, tiled=True)
    rest = lax.all_gather(factor[1:], "col", axis=3, tiled=True)
    panel = jnp.concatenate([first, rest], axis=0)

    width = (steps - 1) * nb
    top = broadcast_halves(first[0, 0, :, :width], n, {k: k for k in range(1, steps)})

    solved = []
    for k in range(steps):
        acc = held[k]
        for j in range(k):
            acc = acc - matmul(top[k][:, j * nb : (j + 1) * nb], solved[j])
        solved.append(matmul(diag_inv[k], acc))
    every = jnp.concatenate(solved, axis=0)
    stacked = jnp.stack(solved)

    flat_panel = panel.reshape(local_blocks * nb, steps * nb)
    update = matmul(flat_panel, every, lax.Precision.HIGH).reshape(rhs.shape)
    work = rhs - update
    blocks = (jnp.arange(local_blocks, dtype=jnp.int32) * n + position)[:, None, None, None]
    mine = stacked[jnp.minimum(position, steps - 1)][None, None]
    return jnp.where(blocks < steps, mine, work)


def solution(mesh):
    return jax.shard_map(
        per_device,
        mesh=mesh,
        in_specs=(P(None, "row", None, "col"), P(None, "row", None, "col"), P()),
        out_specs=P(None, "row", None, "col"),
        check_vma=False,
    )
```

```python
import jax
import jax.numpy as jnp
from jax import lax
from jax.sharding import PartitionSpec as P

PARTS = 4


def matmul(left, right, precision=lax.Precision.HIGHEST):
    return jnp.dot(left, right, precision=precision, preferred_element_type=jnp.float32)


def neighbours(n):
    kinds = [lambda u: u ^ 1, lambda u: u + 2, lambda u: u - 2]
    if n > 8:
        kinds += [lambda u: u + 8, lambda u: u - 8]
    return kinds


def schedule(n, sources):
    have = [set() for _ in range(n)]
    for item, row in sources.items():
        have[row].add(item)
    slots = []
    while any(len(h) < len(sources) for h in have):
        slot, incoming = [], [set() for _ in range(n)]
        for kind in neighbours(n):
            moves = []
            for u in range(n):
                v = kind(u)
                if not 0 <= v < n:
                    continue
                want = sorted(have[u] - have[v] - incoming[v])
                if want:
                    incoming[v].add(want[0])
                    moves.append((u, v, want[0]))
            if moves:
                slot.append(moves)
        for moves in slot:
            for u, v, item in moves:
                have[v].add(item)
        slots.append(slot)
    return slots


def member(rows, n):
    position = lax.axis_index("row")
    found = jnp.zeros((), jnp.bool_)
    for low in range(0, n, 32):
        bits = sum(1 << (u - low) for u in rows if low <= u < low + 32)
        if bits:
            shift = jnp.clip(position - low, 0, 31).astype(jnp.uint32)
            hit = ((jnp.uint32(bits) >> shift) & jnp.uint32(1)) == jnp.uint32(1)
            found = found | (hit & (position >= low) & (position < low + 32))
    return found


def broadcast_chunks(own, n, rows, parts=PARTS):
    width = own.shape[1] // parts
    pieces = broadcast(
        {(k, h): own[:, h * width : (h + 1) * width] for k in rows for h in range(parts)},
        n,
        {(k, h): rows[k] for k in rows for h in range(parts)},
    )
    return {k: jnp.concatenate([pieces[(k, h)] for h in range(parts)], axis=1) for k in rows}


def broadcast(own, n, sources):
    items = dict(own)
    for slot in schedule(n, sources):
        received = []
        for moves in slot:
            senders = {}
            for u, _, item in moves:
                senders.setdefault(item, []).append(u)
            order = sorted(senders)
            payload = items[order[0]]
            for item in order[1:]:
                payload = jnp.where(member(senders[item], n), items[item], payload)
            got = lax.ppermute(payload, "row", [(u, v) for u, v, _ in moves])
            received.append((moves, got))
        for moves, got in received:
            receivers = {}
            for _, v, item in moves:
                receivers.setdefault(item, []).append(v)
            for item, rows in receivers.items():
                items[item] = jnp.where(member(rows, n), got, items[item])
    return items


def per_device(factor, rhs, diag_inv):
    n = lax.axis_size("row")
    steps = diag_inv.shape[0]
    nb = rhs.shape[2]
    local_blocks = rhs.shape[0]
    position = lax.axis_index("row")

    held = broadcast_chunks(rhs[0, 0], n, {k: k for k in range(steps)})

    first = lax.all_gather(factor[:1], "col", axis=3, tiled=True)
    rest = lax.all_gather(factor[1:], "col", axis=3, tiled=True)
    panel = jnp.concatenate([first, rest], axis=0)

    width = (steps - 1) * nb
    top = broadcast_chunks(first[0, 0, :, :width], n, {k: k for k in range(1, steps)})

    solved = []
    for k in range(steps):
        acc = held[k]
        for j in range(k):
            acc = acc - matmul(top[k][:, j * nb : (j + 1) * nb], solved[j])
        solved.append(matmul(diag_inv[k], acc))
    every = jnp.concatenate(solved, axis=0)
    stacked = jnp.stack(solved)

    flat_panel = panel.reshape(local_blocks * nb, steps * nb)
    update = matmul(flat_panel, every, lax.Precision.HIGH).reshape(rhs.shape)
    work = rhs - update
    blocks = (jnp.arange(local_blocks, dtype=jnp.int32) * n + position)[:, None, None, None]
    mine = stacked[jnp.minimum(position, steps - 1)][None, None]
    return jnp.where(blocks < steps, mine, work)


def solution(mesh):
    return jax.shard_map(
        per_device,
        mesh=mesh,
        in_specs=(P(None, "row", None, "col"), P(None, "row", None, "col"), P()),
        out_specs=P(None, "row", None, "col"),
        check_vma=False,
    )
```

```python
import jax
import jax.numpy as jnp
from jax import lax
from jax.sharding import PartitionSpec as P

PARTS = 2


def matmul(left, right, precision=lax.Precision.HIGHEST):
    return jnp.dot(left, right, precision=precision, preferred_element_type=jnp.float32)


def neighbours(n):
    kinds = [lambda u: u ^ 1, lambda u: u + 2, lambda u: u - 2]
    if n > 8:
        kinds += [lambda u: u + 8, lambda u: u - 8]
    return kinds


def schedule(n, sources):
    have = [set() for _ in range(n)]
    for item, row in sources.items():
        have[row].add(item)
    slots = []
    while any(len(h) < len(sources) for h in have):
        slot, incoming = [], [set() for _ in range(n)]
        for kind in neighbours(n):
            moves = []
            for u in range(n):
                v = kind(u)
                if not 0 <= v < n:
                    continue
                want = sorted(have[u] - have[v] - incoming[v])
                if want:
                    incoming[v].add(want[0])
                    moves.append((u, v, want[0]))
            if moves:
                slot.append(moves)
        for moves in slot:
            for u, v, item in moves:
                have[v].add(item)
        slots.append(slot)
    return slots


def member(rows, n):
    position = lax.axis_index("row")
    found = jnp.zeros((), jnp.bool_)
    for low in range(0, n, 32):
        bits = sum(1 << (u - low) for u in rows if low <= u < low + 32)
        if bits:
            shift = jnp.clip(position - low, 0, 31).astype(jnp.uint32)
            hit = ((jnp.uint32(bits) >> shift) & jnp.uint32(1)) == jnp.uint32(1)
            found = found | (hit & (position >= low) & (position < low + 32))
    return found


def broadcast_chunks(own, n, rows, parts=PARTS):
    width = own.shape[1] // parts
    pieces = broadcast(
        {(k, h): own[:, h * width : (h + 1) * width] for k in rows for h in range(parts)},
        n,
        {(k, h): rows[k] for k in rows for h in range(parts)},
    )
    return {k: jnp.concatenate([pieces[(k, h)] for h in range(parts)], axis=1) for k in rows}


def broadcast(own, n, sources):
    items = dict(own)
    for slot in schedule(n, sources):
        received = []
        for moves in slot:
            senders = {}
            for u, _, item in moves:
                senders.setdefault(item, []).append(u)
            order = sorted(senders)
            payload = items[order[0]]
            for item in order[1:]:
                payload = jnp.where(member(senders[item], n), items[item], payload)
            got = lax.ppermute(payload, "row", [(u, v) for u, v, _ in moves])
            received.append((moves, got))
        for moves, got in received:
            receivers = {}
            for _, v, item in moves:
                receivers.setdefault(item, []).append(v)
            for item, rows in receivers.items():
                items[item] = jnp.where(member(rows, n), got, items[item])
    return items


def per_device(factor, rhs, diag_inv):
    n = lax.axis_size("row")
    steps = diag_inv.shape[0]
    nb = rhs.shape[2]
    local_blocks = rhs.shape[0]
    position = lax.axis_index("row")

    held = broadcast_chunks(rhs[0, 0], n, {k: k for k in range(steps)})

    first = lax.all_gather(factor[:1], "col", axis=3, tiled=True)
    rest = lax.all_gather(factor[1:], "col", axis=3, tiled=True)
    panel = jnp.concatenate([first, rest], axis=0)

    width = (steps - 1) * nb
    top = broadcast_chunks(first[0, 0, :, :width], n, {k: k for k in range(1, steps)}, 1)

    solved = []
    for k in range(steps):
        acc = held[k]
        for j in range(k):
            acc = acc - matmul(top[k][:, j * nb : (j + 1) * nb], solved[j])
        solved.append(matmul(diag_inv[k], acc))
    every = jnp.concatenate(solved, axis=0)
    stacked = jnp.stack(solved)

    flat_panel = panel.reshape(local_blocks * nb, steps * nb)
    update = matmul(flat_panel, every, lax.Precision.HIGH).reshape(rhs.shape)
    work = rhs - update
    blocks = (jnp.arange(local_blocks, dtype=jnp.int32) * n + position)[:, None, None, None]
    mine = stacked[jnp.minimum(position, steps - 1)][None, None]
    return jnp.where(blocks < steps, mine, work)


def solution(mesh):
    return jax.shard_map(
        per_device,
        mesh=mesh,
        in_specs=(P(None, "row", None, "col"), P(None, "row", None, "col"), P()),
        out_specs=P(None, "row", None, "col"),
        check_vma=False,
    )
```

```python
import jax
import jax.numpy as jnp
from jax import lax
from jax.sharding import PartitionSpec as P

PARTS = 2


def matmul(left, right, precision=lax.Precision.HIGHEST):
    return jnp.dot(left, right, precision=precision, preferred_element_type=jnp.float32)


def neighbours(n):
    kinds = [lambda u: u ^ 1, lambda u: u + 2, lambda u: u - 2]
    if n > 8:
        kinds += [lambda u: u + 8, lambda u: u - 8]
    return kinds


def schedule(n, sources):
    have = [set() for _ in range(n)]
    for item, row in sources.items():
        have[row].add(item)
    slots = []
    while any(len(h) < len(sources) for h in have):
        slot, incoming = [], [set() for _ in range(n)]
        for kind in neighbours(n):
            moves = []
            for u in range(n):
                v = kind(u)
                if not 0 <= v < n:
                    continue
                want = sorted(have[u] - have[v] - incoming[v])
                if want:
                    incoming[v].add(want[0])
                    moves.append((u, v, want[0]))
            if moves:
                slot.append(moves)
        for moves in slot:
            for u, v, item in moves:
                have[v].add(item)
        slots.append(slot)
    return slots


def member(rows, n):
    position = lax.axis_index("row")
    found = jnp.zeros((), jnp.bool_)
    for low in range(0, n, 32):
        bits = sum(1 << (u - low) for u in rows if low <= u < low + 32)
        if bits:
            shift = jnp.clip(position - low, 0, 31).astype(jnp.uint32)
            hit = ((jnp.uint32(bits) >> shift) & jnp.uint32(1)) == jnp.uint32(1)
            found = found | (hit & (position >= low) & (position < low + 32))
    return found


def broadcast_chunks(own, n, rows, parts=PARTS):
    width = own.shape[1] // parts
    pieces = broadcast(
        {(k, h): own[:, h * width : (h + 1) * width] for k in rows for h in range(parts)},
        n,
        {(k, h): rows[k] for k in rows for h in range(parts)},
    )
    return {k: jnp.concatenate([pieces[(k, h)] for h in range(parts)], axis=1) for k in rows}


def broadcast(own, n, sources):
    items = dict(own)
    for slot in schedule(n, sources):
        received = []
        for moves in slot:
            senders = {}
            for u, _, item in moves:
                senders.setdefault(item, []).append(u)
            order = sorted(senders)
            payload = items[order[0]]
            for item in order[1:]:
                payload = jnp.where(member(senders[item], n), items[item], payload)
            got = lax.ppermute(payload, "row", [(u, v) for u, v, _ in moves])
            received.append((moves, got))
        for moves, got in received:
            receivers = {}
            for _, v, item in moves:
                receivers.setdefault(item, []).append(v)
            for item, rows in receivers.items():
                items[item] = jnp.where(member(rows, n), got, items[item])
    return items


def per_device(factor, rhs, diag_inv):
    n = lax.axis_size("row")
    steps = diag_inv.shape[0]
    nb = rhs.shape[2]
    local_blocks = rhs.shape[0]
    position = lax.axis_index("row")

    held = broadcast_chunks(rhs[0, 0], n, {k: k for k in range(steps)})

    first = lax.all_gather(factor[:1], "col", axis=3, tiled=True)
    rest = lax.all_gather(factor[1:], "col", axis=3, tiled=True)
    panel = jnp.concatenate([first, rest], axis=0)

    lower = {(k, j): first[0, 0, :, j * nb : (j + 1) * nb] for k in range(1, steps) for j in range(k)}
    top = broadcast(lower, n, {(k, j): k for k, j in lower})

    solved = []
    for k in range(steps):
        acc = held[k]
        for j in range(k):
            acc = acc - matmul(top[(k, j)], solved[j])
        solved.append(matmul(diag_inv[k], acc))
    every = jnp.concatenate(solved, axis=0)
    stacked = jnp.stack(solved)

    flat_panel = panel.reshape(local_blocks * nb, steps * nb)
    update = matmul(flat_panel, every, lax.Precision.HIGH).reshape(rhs.shape)
    work = rhs - update
    blocks = (jnp.arange(local_blocks, dtype=jnp.int32) * n + position)[:, None, None, None]
    mine = stacked[jnp.minimum(position, steps - 1)][None, None]
    return jnp.where(blocks < steps, mine, work)


def solution(mesh):
    return jax.shard_map(
        per_device,
        mesh=mesh,
        in_specs=(P(None, "row", None, "col"), P(None, "row", None, "col"), P()),
        out_specs=P(None, "row", None, "col"),
        check_vma=False,
    )
```

```python
import jax
import jax.numpy as jnp
from jax import lax
from jax.sharding import PartitionSpec as P

PARTS = 2


def matmul(left, right, precision=lax.Precision.HIGHEST):
    return jnp.dot(left, right, precision=precision, preferred_element_type=jnp.float32)


def neighbours(n):
    kinds = [lambda u: u ^ 1, lambda u: u + 2, lambda u: u - 2]
    if n > 8:
        kinds += [lambda u: u + 8, lambda u: u - 8]
    return kinds


def schedule(n, sources):
    have = [set() for _ in range(n)]
    for item, row in sources.items():
        have[row].add(item)
    slots = []
    while any(len(h) < len(sources) for h in have):
        slot, incoming = [], [set() for _ in range(n)]
        holders = {item: sum(item in h for h in have) for item in sources}
        for kind in neighbours(n):
            moves = []
            for u in range(n):
                v = kind(u)
                if not 0 <= v < n:
                    continue
                want = sorted(have[u] - have[v] - incoming[v], key=lambda item: (holders[item], item))
                if want:
                    incoming[v].add(want[0])
                    moves.append((u, v, want[0]))
            if moves:
                slot.append(moves)
        for moves in slot:
            for u, v, item in moves:
                have[v].add(item)
        slots.append(slot)
    return slots


def member(rows, n):
    position = lax.axis_index("row")
    found = jnp.zeros((), jnp.bool_)
    for low in range(0, n, 32):
        bits = sum(1 << (u - low) for u in rows if low <= u < low + 32)
        if bits:
            shift = jnp.clip(position - low, 0, 31).astype(jnp.uint32)
            hit = ((jnp.uint32(bits) >> shift) & jnp.uint32(1)) == jnp.uint32(1)
            found = found | (hit & (position >= low) & (position < low + 32))
    return found


def broadcast_chunks(own, n, rows, parts=PARTS):
    width = own.shape[1] // parts
    pieces = broadcast(
        {(k, h): own[:, h * width : (h + 1) * width] for k in rows for h in range(parts)},
        n,
        {(k, h): rows[k] for k in rows for h in range(parts)},
    )
    return {k: jnp.concatenate([pieces[(k, h)] for h in range(parts)], axis=1) for k in rows}


def broadcast(own, n, sources):
    items = dict(own)
    for slot in schedule(n, sources):
        received = []
        for moves in slot:
            senders = {}
            for u, _, item in moves:
                senders.setdefault(item, []).append(u)
            order = sorted(senders)
            payload = items[order[0]]
            for item in order[1:]:
                payload = jnp.where(member(senders[item], n), items[item], payload)
            got = lax.ppermute(payload, "row", [(u, v) for u, v, _ in moves])
            received.append((moves, got))
        for moves, got in received:
            receivers = {}
            for _, v, item in moves:
                receivers.setdefault(item, []).append(v)
            for item, rows in receivers.items():
                items[item] = jnp.where(member(rows, n), got, items[item])
    return items


def per_device(factor, rhs, diag_inv):
    n = lax.axis_size("row")
    steps = diag_inv.shape[0]
    nb = rhs.shape[2]
    local_blocks = rhs.shape[0]
    position = lax.axis_index("row")

    held = broadcast_chunks(rhs[0, 0], n, {k: k for k in range(steps)})

    first = lax.all_gather(factor[:1], "col", axis=3, tiled=True)
    rest = lax.all_gather(factor[1:], "col", axis=3, tiled=True)
    panel = jnp.concatenate([first, rest], axis=0)

    lower = {(k, j): first[0, 0, :, j * nb : (j + 1) * nb] for k in range(1, steps) for j in range(k)}
    top = broadcast(lower, n, {(k, j): k for k, j in lower})

    solved = []
    for k in range(steps):
        acc = held[k]
        for j in range(k):
            acc = acc - matmul(top[(k, j)], solved[j])
        solved.append(matmul(diag_inv[k], acc))
    every = jnp.concatenate(solved, axis=0)
    stacked = jnp.stack(solved)

    flat_panel = panel.reshape(local_blocks * nb, steps * nb)
    update = matmul(flat_panel, every, lax.Precision.HIGH).reshape(rhs.shape)
    work = rhs - update
    blocks = (jnp.arange(local_blocks, dtype=jnp.int32) * n + position)[:, None, None, None]
    mine = stacked[jnp.minimum(position, steps - 1)][None, None]
    return jnp.where(blocks < steps, mine, work)


def solution(mesh):
    return jax.shard_map(
        per_device,
        mesh=mesh,
        in_specs=(P(None, "row", None, "col"), P(None, "row", None, "col"), P()),
        out_specs=P(None, "row", None, "col"),
        check_vma=False,
    )
```

```python
import jax
import jax.numpy as jnp
from jax import lax
from jax.sharding import PartitionSpec as P

PARTS = 2


def matmul(left, right, precision=lax.Precision.HIGHEST):
    return jnp.dot(left, right, precision=precision, preferred_element_type=jnp.float32)


def neighbours(n):
    kinds = [lambda u: u ^ 1, lambda u: u + 2, lambda u: u - 2]
    if n > 8:
        kinds += [lambda u: u + 8, lambda u: u - 8]
    return kinds


def schedule(n, sources):
    have = [set() for _ in range(n)]
    for item, row in sources.items():
        have[row].add(item)
    slots = []
    while any(len(h) < len(sources) for h in have):
        slot, incoming = [], [set() for _ in range(n)]
        holders = {item: sum(item in h for h in have) for item in sources}
        for kind in neighbours(n):
            moves = []
            for u in range(n):
                v = kind(u)
                if not 0 <= v < n:
                    continue
                want = sorted(have[u] - have[v] - incoming[v], key=lambda item: (holders[item], item))
                if want:
                    incoming[v].add(want[0])
                    moves.append((u, v, want[0]))
            if moves:
                slot.append(moves)
        for moves in slot:
            for u, v, item in moves:
                have[v].add(item)
        slots.append(slot)
    return slots


def member(rows, n):
    position = lax.axis_index("row")
    found = jnp.zeros((), jnp.bool_)
    for low in range(0, n, 32):
        bits = sum(1 << (u - low) for u in rows if low <= u < low + 32)
        if bits:
            shift = jnp.clip(position - low, 0, 31).astype(jnp.uint32)
            hit = ((jnp.uint32(bits) >> shift) & jnp.uint32(1)) == jnp.uint32(1)
            found = found | (hit & (position >= low) & (position < low + 32))
    return found


def broadcast_chunks(own, n, rows, parts=PARTS):
    width = own.shape[1] // parts
    pieces = broadcast(
        {(k, h): own[:, h * width : (h + 1) * width] for k in rows for h in range(parts)},
        n,
        {(k, h): rows[k] for k in rows for h in range(parts)},
    )
    return {k: jnp.concatenate([pieces[(k, h)] for h in range(parts)], axis=1) for k in rows}


def broadcast(own, n, sources):
    items = dict(own)
    for slot in schedule(n, sources):
        received = []
        for moves in slot:
            senders = {}
            for u, _, item in moves:
                senders.setdefault(item, []).append(u)
            order = sorted(senders)
            payload = items[order[0]]
            for item in order[1:]:
                payload = jnp.where(member(senders[item], n), items[item], payload)
            got = lax.ppermute(payload, "row", [(u, v) for u, v, _ in moves])
            received.append((moves, got))
        for moves, got in received:
            receivers = {}
            for _, v, item in moves:
                receivers.setdefault(item, []).append(v)
            for item, rows in receivers.items():
                items[item] = jnp.where(member(rows, n), got, items[item])
    return items


def per_device(factor, rhs, diag_inv):
    n = lax.axis_size("row")
    steps = diag_inv.shape[0]
    nb = rhs.shape[2]
    local_blocks = rhs.shape[0]
    position = lax.axis_index("row")

    held = broadcast_chunks(rhs[0, 0], n, {k: k for k in range(steps)})

    first = lax.all_gather(factor[:1], "col", axis=3, tiled=True)
    rest = lax.all_gather(factor[1:], "col", axis=3, tiled=True)
    panel = jnp.concatenate([first, rest], axis=0)

    lower = {(k, j): first[0, 0, :, j * nb : (j + 1) * nb] for k in range(1, steps) for j in range(k)}
    top = broadcast(lower, n, {(k, j): k for k, j in lower})

    solved = []
    for k in range(steps):
        acc = held[k]
        for j in range(k):
            acc = acc - matmul(top[(k, j)], solved[j])
        solved.append(matmul(diag_inv[k], acc))
    every = jnp.concatenate(solved, axis=0)
    stacked = jnp.stack(solved)

    flat_panel = panel.reshape(local_blocks * nb, steps * nb)
    update = matmul(flat_panel, every, lax.Precision.HIGH).reshape(rhs.shape)
    work = rhs - update
    head = jnp.where(position < steps, stacked[jnp.minimum(position, steps - 1)], work[0, 0])
    return work.at[0, 0].set(head)


def solution(mesh):
    return jax.shard_map(
        per_device,
        mesh=mesh,
        in_specs=(P(None, "row", None, "col"), P(None, "row", None, "col"), P()),
        out_specs=P(None, "row", None, "col"),
        check_vma=False,
    )
```

```python
import jax
import jax.numpy as jnp
from jax import lax
from jax.sharding import PartitionSpec as P

PARTS = 2


def matmul(left, right, precision=lax.Precision.HIGHEST):
    return jnp.dot(left, right, precision=precision, preferred_element_type=jnp.float32)


def neighbours(n):
    kinds = [lambda u: u + 2, lambda u: u - 2, lambda u: u ^ 1]
    if n > 8:
        kinds += [lambda u: u + 8, lambda u: u - 8]
    return kinds


def schedule(n, sources):
    have = [set() for _ in range(n)]
    for item, row in sources.items():
        have[row].add(item)
    slots = []
    while any(len(h) < len(sources) for h in have):
        slot, incoming = [], [set() for _ in range(n)]
        holders = {item: sum(item in h for h in have) for item in sources}
        for kind in neighbours(n):
            moves = []
            for u in range(n):
                v = kind(u)
                if not 0 <= v < n:
                    continue
                want = sorted(have[u] - have[v] - incoming[v], key=lambda item: (holders[item], item))
                if want:
                    incoming[v].add(want[0])
                    moves.append((u, v, want[0]))
            if moves:
                slot.append(moves)
        for moves in slot:
            for u, v, item in moves:
                have[v].add(item)
        slots.append(slot)
    return slots


def member(rows, n):
    position = lax.axis_index("row")
    found = jnp.zeros((), jnp.bool_)
    for low in range(0, n, 32):
        bits = sum(1 << (u - low) for u in rows if low <= u < low + 32)
        if bits:
            shift = jnp.clip(position - low, 0, 31).astype(jnp.uint32)
            hit = ((jnp.uint32(bits) >> shift) & jnp.uint32(1)) == jnp.uint32(1)
            found = found | (hit & (position >= low) & (position < low + 32))
    return found


def broadcast_chunks(own, n, rows, parts=PARTS):
    width = own.shape[1] // parts
    pieces = broadcast(
        {(k, h): own[:, h * width : (h + 1) * width] for k in rows for h in range(parts)},
        n,
        {(k, h): rows[k] for k in rows for h in range(parts)},
    )
    return {k: jnp.concatenate([pieces[(k, h)] for h in range(parts)], axis=1) for k in rows}


def broadcast(own, n, sources):
    items = dict(own)
    for slot in schedule(n, sources):
        received = []
        for moves in slot:
            senders = {}
            for u, _, item in moves:
                senders.setdefault(item, []).append(u)
            order = sorted(senders)
            payload = items[order[0]]
            for item in order[1:]:
                payload = jnp.where(member(senders[item], n), items[item], payload)
            got = lax.ppermute(payload, "row", [(u, v) for u, v, _ in moves])
            received.append((moves, got))
        for moves, got in received:
            receivers = {}
            for _, v, item in moves:
                receivers.setdefault(item, []).append(v)
            for item, rows in receivers.items():
                items[item] = jnp.where(member(rows, n), got, items[item])
    return items


def per_device(factor, rhs, diag_inv):
    n = lax.axis_size("row")
    steps = diag_inv.shape[0]
    nb = rhs.shape[2]
    local_blocks = rhs.shape[0]
    position = lax.axis_index("row")

    held = broadcast_chunks(rhs[0, 0], n, {k: k for k in range(steps)})

    first = lax.all_gather(factor[:1], "col", axis=3, tiled=True)
    rest = lax.all_gather(factor[1:], "col", axis=3, tiled=True)
    panel = jnp.concatenate([first, rest], axis=0)

    lower = {(k, j): first[0, 0, :, j * nb : (j + 1) * nb] for k in range(1, steps) for j in range(k)}
    top = broadcast(lower, n, {(k, j): k for k, j in lower})

    solved = []
    for k in range(steps):
        acc = held[k]
        for j in range(k):
            acc = acc - matmul(top[(k, j)], solved[j])
        solved.append(matmul(diag_inv[k], acc))
    every = jnp.concatenate(solved, axis=0)
    stacked = jnp.stack(solved)

    flat_panel = panel.reshape(local_blocks * nb, steps * nb)
    update = matmul(flat_panel, every, lax.Precision.HIGH).reshape(rhs.shape)
    work = rhs - update
    head = jnp.where(position < steps, stacked[jnp.minimum(position, steps - 1)], work[0, 0])
    return work.at[0, 0].set(head)


def solution(mesh):
    return jax.shard_map(
        per_device,
        mesh=mesh,
        in_specs=(P(None, "row", None, "col"), P(None, "row", None, "col"), P()),
        out_specs=P(None, "row", None, "col"),
        check_vma=False,
    )
```

```python
import jax
import jax.numpy as jnp
from jax import lax
from jax.sharding import PartitionSpec as P

PARTS = 2


def matmul(left, right, precision=lax.Precision.HIGHEST):
    return jnp.dot(left, right, precision=precision, preferred_element_type=jnp.float32)


def neighbours(n):
    kinds = [lambda u: u ^ 1, lambda u: u - 2, lambda u: u + 2]
    if n > 8:
        kinds += [lambda u: u + 8, lambda u: u - 8]
    return kinds


def schedule(n, sources):
    have = [set() for _ in range(n)]
    for item, row in sources.items():
        have[row].add(item)
    slots = []
    while any(len(h) < len(sources) for h in have):
        slot, incoming = [], [set() for _ in range(n)]
        holders = {item: sum(item in h for h in have) for item in sources}
        for kind in neighbours(n):
            moves = []
            for u in range(n):
                v = kind(u)
                if not 0 <= v < n:
                    continue
                want = sorted(have[u] - have[v] - incoming[v], key=lambda item: (holders[item], item))
                if want:
                    incoming[v].add(want[0])
                    moves.append((u, v, want[0]))
            if moves:
                slot.append(moves)
        for moves in slot:
            for u, v, item in moves:
                have[v].add(item)
        slots.append(slot)
    return slots


def member(rows, n):
    position = lax.axis_index("row")
    found = jnp.zeros((), jnp.bool_)
    for low in range(0, n, 32):
        bits = sum(1 << (u - low) for u in rows if low <= u < low + 32)
        if bits:
            shift = jnp.clip(position - low, 0, 31).astype(jnp.uint32)
            hit = ((jnp.uint32(bits) >> shift) & jnp.uint32(1)) == jnp.uint32(1)
            found = found | (hit & (position >= low) & (position < low + 32))
    return found


def broadcast_chunks(own, n, rows, parts=PARTS):
    width = own.shape[1] // parts
    pieces = broadcast(
        {(k, h): own[:, h * width : (h + 1) * width] for k in rows for h in range(parts)},
        n,
        {(k, h): rows[k] for k in rows for h in range(parts)},
    )
    return {k: jnp.concatenate([pieces[(k, h)] for h in range(parts)], axis=1) for k in rows}


def broadcast(own, n, sources):
    items = dict(own)
    for slot in schedule(n, sources):
        received = []
        for moves in slot:
            senders = {}
            for u, _, item in moves:
                senders.setdefault(item, []).append(u)
            order = sorted(senders)
            payload = items[order[0]]
            for item in order[1:]:
                payload = jnp.where(member(senders[item], n), items[item], payload)
            got = lax.ppermute(payload, "row", [(u, v) for u, v, _ in moves])
            received.append((moves, got))
        for moves, got in received:
            receivers = {}
            for _, v, item in moves:
                receivers.setdefault(item, []).append(v)
            for item, rows in receivers.items():
                items[item] = jnp.where(member(rows, n), got, items[item])
    return items


def per_device(factor, rhs, diag_inv):
    n = lax.axis_size("row")
    steps = diag_inv.shape[0]
    nb = rhs.shape[2]
    local_blocks = rhs.shape[0]
    position = lax.axis_index("row")

    held = broadcast_chunks(rhs[0, 0], n, {k: k for k in range(steps)})

    first = lax.all_gather(factor[:1], "col", axis=3, tiled=True)
    rest = lax.all_gather(factor[1:], "col", axis=3, tiled=True)
    panel = jnp.concatenate([first, rest], axis=0)

    lower = {(k, j): first[0, 0, :, j * nb : (j + 1) * nb] for k in range(1, steps) for j in range(k)}
    top = broadcast(lower, n, {(k, j): k for k, j in lower})

    solved = []
    for k in range(steps):
        acc = held[k]
        for j in range(k):
            acc = acc - matmul(top[(k, j)], solved[j])
        solved.append(matmul(diag_inv[k], acc))
    every = jnp.concatenate(solved, axis=0)
    stacked = jnp.stack(solved)

    flat_panel = panel.reshape(local_blocks * nb, steps * nb)
    update = matmul(flat_panel, every, lax.Precision.HIGH).reshape(rhs.shape)
    work = rhs - update
    head = jnp.where(position < steps, stacked[jnp.minimum(position, steps - 1)], work[0, 0])
    return work.at[0, 0].set(head)


def solution(mesh):
    return jax.shard_map(
        per_device,
        mesh=mesh,
        in_specs=(P(None, "row", None, "col"), P(None, "row", None, "col"), P()),
        out_specs=P(None, "row", None, "col"),
        check_vma=False,
    )
```

```python
import jax
import jax.numpy as jnp
from jax import lax
from jax.sharding import PartitionSpec as P

PARTS = 2


def matmul(left, right, precision=lax.Precision.HIGHEST):
    return jnp.dot(left, right, precision=precision, preferred_element_type=jnp.float32)


def neighbours(n):
    kinds = [lambda u: u + 2, lambda u: u ^ 1, lambda u: u - 2]
    if n > 8:
        kinds += [lambda u: u + 8, lambda u: u - 8]
    return kinds


def schedule(n, sources):
    have = [set() for _ in range(n)]
    for item, row in sources.items():
        have[row].add(item)
    slots = []
    while any(len(h) < len(sources) for h in have):
        slot, incoming = [], [set() for _ in range(n)]
        holders = {item: sum(item in h for h in have) for item in sources}
        for kind in neighbours(n):
            moves = []
            for u in range(n):
                v = kind(u)
                if not 0 <= v < n:
                    continue
                want = sorted(have[u] - have[v] - incoming[v], key=lambda item: (holders[item], item))
                if want:
                    incoming[v].add(want[0])
                    moves.append((u, v, want[0]))
            if moves:
                slot.append(moves)
        for moves in slot:
            for u, v, item in moves:
                have[v].add(item)
        slots.append(slot)
    return slots


def member(rows, n):
    position = lax.axis_index("row")
    found = jnp.zeros((), jnp.bool_)
    for low in range(0, n, 32):
        bits = sum(1 << (u - low) for u in rows if low <= u < low + 32)
        if bits:
            shift = jnp.clip(position - low, 0, 31).astype(jnp.uint32)
            hit = ((jnp.uint32(bits) >> shift) & jnp.uint32(1)) == jnp.uint32(1)
            found = found | (hit & (position >= low) & (position < low + 32))
    return found


def broadcast_chunks(own, n, rows, parts=PARTS):
    width = own.shape[1] // parts
    pieces = broadcast(
        {(k, h): own[:, h * width : (h + 1) * width] for k in rows for h in range(parts)},
        n,
        {(k, h): rows[k] for k in rows for h in range(parts)},
    )
    return {k: jnp.concatenate([pieces[(k, h)] for h in range(parts)], axis=1) for k in rows}


def broadcast(own, n, sources):
    items = dict(own)
    for slot in schedule(n, sources):
        received = []
        for moves in slot:
            senders = {}
            for u, _, item in moves:
                senders.setdefault(item, []).append(u)
            order = sorted(senders)
            payload = items[order[0]]
            for item in order[1:]:
                payload = jnp.where(member(senders[item], n), items[item], payload)
            got = lax.ppermute(payload, "row", [(u, v) for u, v, _ in moves])
            received.append((moves, got))
        for moves, got in received:
            receivers = {}
            for _, v, item in moves:
                receivers.setdefault(item, []).append(v)
            for item, rows in receivers.items():
                items[item] = jnp.where(member(rows, n), got, items[item])
    return items


def per_device(factor, rhs, diag_inv):
    n = lax.axis_size("row")
    steps = diag_inv.shape[0]
    nb = rhs.shape[2]
    local_blocks = rhs.shape[0]
    position = lax.axis_index("row")

    held = broadcast_chunks(rhs[0, 0], n, {k: k for k in range(steps)})

    first = lax.all_gather(factor[:1], "col", axis=3, tiled=True)
    rest = lax.all_gather(factor[1:], "col", axis=3, tiled=True)
    panel = jnp.concatenate([first, rest], axis=0)

    lower = {(k, j): first[0, 0, :, j * nb : (j + 1) * nb] for k in range(1, steps) for j in range(k)}
    top = broadcast(lower, n, {(k, j): k for k, j in lower})

    solved = []
    for k in range(steps):
        acc = held[k]
        for j in range(k):
            acc = acc - matmul(top[(k, j)], solved[j])
        solved.append(matmul(diag_inv[k], acc))
    every = jnp.concatenate(solved, axis=0)
    stacked = jnp.stack(solved)

    flat_panel = panel.reshape(local_blocks * nb, steps * nb)
    update = matmul(flat_panel, every, lax.Precision.HIGH).reshape(rhs.shape)
    work = rhs - update
    head = jnp.where(position < steps, stacked[jnp.minimum(position, steps - 1)], work[0, 0])
    return work.at[0, 0].set(head)


def solution(mesh):
    return jax.shard_map(
        per_device,
        mesh=mesh,
        in_specs=(P(None, "row", None, "col"), P(None, "row", None, "col"), P()),
        out_specs=P(None, "row", None, "col"),
        check_vma=False,
    )
```
